128 devices in a mesh: sens: 16 (over x, y_lo, core), freq: 8 (over z, y_hi).
Axes of the slice: x: 4, y: 4 (y_hi: 2, y_lo: 2; y = y_hi * 2 + y_lo), z: 4, core: 2. Of those that a mesh axis runs over, the one named last changes fastest.
Arguments:
- residual: bfloat16 [131072, 2048], P('sens', 'freq'), may hold values from -6 to 6
- spec_gain: float32 [1025], replicated, may hold values from 0.3 to 3
- factor_panel: bfloat16 [131072, 3072], P(('sens', 'freq')), may hold values from -0.1875 to 0.1875
- diag_inverse: bfloat16 [3072, 1024], replicated, as said below
Outputs:
- whitened: bfloat16 [131072, 2048], P(('sens', 'freq'))
The draws below stay inside these ranges and needn't reach their ends.
Inputs may be any that keep to these rules, and one draw needn't show every extreme that they name: `diag_inverse`: each stacked block of 1024 rows is lower triangular with a positive diagonal.
All inputs are finite; a program needn't handle non-finite values.
Results may differ from the reference program's by a relative error of at most 0.015.
Values may be sent and summed in bfloat16 or wider, within the bound.
No kernel may reach another device: no remote copies, remote signals or barrier semaphores. Data moves between devices by JAX's collectives and lax.ppermute only.
A program may use at most 128 MiB of HBM per device.

```python
import math
import jax
import jax.numpy as jnp
from jax import lax

BLOCK = 1024
NT = 2048
STEPS = 3
SENSORS = 131072


def draw_diag_inverse(key, part):
    key_diag, key_low = jax.random.split(jax.random.fold_in(key, 7))
    rows = jnp.arange(STEPS * BLOCK) % BLOCK
    cols = jnp.arange(BLOCK)
    diag = jnp.exp(jax.random.uniform(key_diag, (STEPS * BLOCK, 1), minval=math.log(0.5), maxval=math.log(2.0)))
    lower = jax.random.normal(key_low, (STEPS * BLOCK, BLOCK)) * (0.6 / math.sqrt(BLOCK))
    on_diag = rows[:, None] == cols[None, :]
    below = rows[:, None] > cols[None, :]
    value = jnp.where(on_diag, diag, jnp.where(below, lower, 0.0))
    return value.astype(jnp.float32).astype(jnp.bfloat16)


def block_levels(key, dims, pieces, low, top_value):
    level, own = 1.0, jax.random.fold_in(key, 6)
    for dim, shards_of in pieces:
        draws = jnp.exp(jax.random.uniform(jax.random.fold_in(own, dim), (shards_of,), jnp.float32, low / len(pieces), top_value / len(pieces)))
        level = level * jnp.repeat(draws, dims[dim] // shards_of).reshape([-1 if axis == dim else 1 for axis in range(len(dims))])
    return level


def normal_values(rng, extent, width, bound, cuts=(), held_as=jnp.bfloat16):
    array = width * jax.random.normal(rng, extent, jnp.float32)
    if cuts:
        array = array * block_levels(rng, extent, cuts, -0.22, 0.18)
    return jnp.clip(array, -bound, bound).astype(held_as)


def setup_inputs(seed: int = 0) -> dict:
    arg_keys = jax.random.split(jax.random.key(seed), 5)
    residual = normal_values(arg_keys[0], (SENSORS, NT), 1.0, 6.0, ((0, 16), (1, 8)))
    spec_gain = jnp.clip(jnp.exp(jax.random.uniform(arg_keys[1], (NT // 2 + 1,), jnp.float32, math.log(0.3), math.log(3.0))), 0.3, 3.0)
    factor_panel = normal_values(arg_keys[2], (SENSORS, STEPS * BLOCK), BLOCK ** -0.5, 0.1875, ((0, 128),))
    diag_inverse = draw_diag_inverse(jax.random.fold_in(arg_keys[4], 71), 0)
    return dict(residual=residual, spec_gain=spec_gain, factor_panel=factor_panel, diag_inverse=diag_inverse)


def kernel_matrix(spec_gain):
    taps = jnp.fft.irfft(spec_gain, n=NT)
    offsets = (jnp.arange(NT)[None, :] - jnp.arange(NT)[:, None]) % NT
    return taps[offsets].astype(jnp.bfloat16)


def reference(residual, spec_gain, factor_panel, diag_inverse):
    hi = lax.Precision.HIGHEST
    kernel = kernel_matrix(spec_gain).astype(jnp.float32)

    def filtered(rows):
        return jnp.dot(rows.astype(jnp.float32), kernel, precision=hi)

    head = filtered(residual[: STEPS * BLOCK])
    solved = []
    for step in range(STEPS):
        field = head[step * BLOCK:(step + 1) * BLOCK]
        for prior in range(step):
            panel = factor_panel[step * BLOCK:(step + 1) * BLOCK, prior * BLOCK:(prior + 1) * BLOCK].astype(jnp.float32)
            field = field - jnp.dot(panel, solved[prior].astype(jnp.float32), precision=hi)
        inverse = diag_inverse[step * BLOCK:(step + 1) * BLOCK].astype(jnp.float32)
        rounded = lax.optimization_barrier(field.astype(jnp.bfloat16))
        solved.append(jnp.dot(inverse, rounded.astype(jnp.float32), precision=hi).astype(jnp.bfloat16))
    rest_rows = residual[STEPS * BLOCK:].reshape(-1, BLOCK, NT)
    rest_panel = factor_panel[STEPS * BLOCK:].reshape(-1, BLOCK, STEPS * BLOCK)

    def one_block(pair):
        rows, panel = pair
        field = filtered(rows)
        for prior in range(STEPS):
            part = panel[:, prior * BLOCK:(prior + 1) * BLOCK].astype(jnp.float32)
            field = field - jnp.dot(part, solved[prior].astype(jnp.float32), precision=hi)
        return field.astype(jnp.bfloat16)

    rest = lax.map(one_block, (rest_rows, rest_panel)).reshape(-1, NT)
    return jnp.concatenate(solved + [rest], axis=0)
```

```python
import jax
import jax.numpy as jnp
from jax import lax
from jax.sharding import PartitionSpec as P

STEPS = 3
ALL = ("sens", "freq")


def circulant(taps):
    n = taps.shape[0]
    nb = 128
    row = lax.broadcasted_iota(jnp.int32, (nb, n), 0)
    band = jnp.broadcast_to(taps[None, :], (nb, n))
    for bit in range(7):
        band = jnp.where(((row >> bit) & 1) == 1, jnp.roll(band, 1 << bit, axis=1), band)
    band = band.astype(jnp.bfloat16)
    return jnp.concatenate([jnp.roll(band, nb * a, axis=1) for a in range(n // nb)], axis=0)


def rotate_to_source(stacked, me, count):
    order = (me - jnp.arange(count)) % count
    return jnp.take(stacked, order, axis=0)


def local(residual, spec_gain, factor_panel, diag_inverse):
    nf = lax.axis_size("freq")
    ns = lax.axis_size("sens")
    fi = lax.axis_index("freq")
    si = lax.axis_index("sens")
    pos = si * nf + fi
    block = factor_panel.shape[0]
    tl = residual.shape[1]
    n = tl * nf
    head = STEPS * block
    f32, bf16 = jnp.float32, jnp.bfloat16

    taps = jnp.fft.irfft(spec_gain, n=n).astype(f32)
    kernel = circulant(taps)

    own = lax.all_to_all(residual, "freq", split_axis=0, concat_axis=1, tiled=True)
    field = jnp.dot(own, kernel, preferred_element_type=f32)

    piece = block // nf
    cols = (STEPS - 1) * block
    got = []
    for d in range(1, nf):
        start = ((fi + d) % nf) * piece
        mine = lax.dynamic_slice_in_dim(factor_panel, start, piece, axis=0)[:, :cols]
        pairs = [(src, (src + d) % nf) for src in range(1, STEPS)]
        got.append(lax.ppermute(mine, ALL, pairs))
    own_piece = lax.dynamic_slice_in_dim(factor_panel, fi * piece, piece, axis=0)[:, :cols]
    part1 = jnp.where(fi == 1, own_piece, 0).astype(bf16)
    part2 = jnp.where(fi == 2, own_piece, 0).astype(bf16)
    for d in range(1, nf):
        part1 = part1 + jnp.where(fi == (1 + d) % nf, got[d - 1], 0).astype(bf16)
        part2 = part2 + jnp.where(fi == (2 + d) % nf, got[d - 1], 0).astype(bf16)
    mixed = jnp.concatenate([part1[:, :block], part2], axis=1)
    stacked = [mixed]
    for d in range(1, nf):
        pairs = [(j, (j + d) % nf) for j in range(nf)]
        stacked.append(lax.ppermute(mixed, ALL, pairs))
    panels = rotate_to_source(jnp.stack(stacked), fi, nf).reshape(nf * piece, STEPS * block)
    p10 = panels[:, :block]
    p20 = panels[:, block : 2 * block]
    p21 = panels[:, 2 * block :]

    rows = [residual[k * block : (k + 1) * block] for k in range(STEPS)]
    inv = [diag_inverse[k * block : (k + 1) * block] for k in range(STEPS)]
    y0 = jnp.dot(inv[0], rows[0], preferred_element_type=f32).astype(bf16)
    z1 = rows[1].astype(f32) - jnp.dot(p10, y0, preferred_element_type=f32)
    y1 = jnp.dot(inv[1], z1.astype(bf16), preferred_element_type=f32).astype(bf16)
    z2 = (
        rows[2].astype(f32)
        - jnp.dot(p20, y0, preferred_element_type=f32)
        - jnp.dot(p21, y1, preferred_element_type=f32)
    )
    y2 = jnp.dot(inv[2], z2.astype(bf16), preferred_element_type=f32).astype(bf16)
    ys = jnp.concatenate([y0, y1, y2], axis=0)

    rp = head // (ns * nf)
    ys4 = ys.reshape(ns, nf, rp, tl)
    got = [lax.dynamic_index_in_dim(ys4, fi, axis=1, keepdims=False)]
    for d in range(1, nf):
        sent = lax.dynamic_index_in_dim(ys4, (fi + d) % nf, axis=1, keepdims=False)
        got.append(lax.ppermute(sent, ALL, [(j, (j + d) % nf) for j in range(nf)]))
    ycol = rotate_to_source(jnp.stack(got), fi, nf)
    ycol = jnp.transpose(ycol, (1, 2, 0, 3)).reshape(ns, rp, n)
    mine = ycol[0]
    for s in range(1, ns):
        recv = lax.ppermute(ycol[s], ALL, [(f, s * nf + f) for f in range(nf)])
        mine = jnp.where(si == s, recv, mine)
    srows = jnp.dot(mine, kernel, preferred_element_type=f32).astype(bf16)
    solved = lax.all_gather(srows, ALL, axis=0, tiled=True)

    update = jnp.dot(factor_panel, solved, preferred_element_type=f32)
    rest = (field - update).astype(bf16)
    step_rows = lax.dynamic_slice_in_dim(solved, jnp.minimum(pos, STEPS - 1) * block, block, axis=0)
    return jnp.where(pos < STEPS, step_rows, rest)


def solution(mesh):
    in_specs = (P("sens", "freq"), P(), P(("sens", "freq"), None), P())
    out_specs = P(("sens", "freq"), None)
    return jax.shard_map(local, mesh=mesh, in_specs=in_specs, out_specs=out_specs, check_vma=False)
```

```python
import jax
import jax.numpy as jnp
from jax import lax
from jax.sharding import PartitionSpec as P

STEPS = 3
ALL = ("sens", "freq")


def circulant(taps):
    n = taps.shape[0]
    nb = 128
    row = lax.broadcasted_iota(jnp.int32, (nb, n), 0)
    band = jnp.broadcast_to(taps[None, :], (nb, n))
    for bit in range(7):
        band = jnp.where(((row >> bit) & 1) == 1, jnp.roll(band, 1 << bit, axis=1), band)
    band = band.astype(jnp.bfloat16)
    return jnp.concatenate([jnp.roll(band, nb * a, axis=1) for a in range(n // nb)], axis=0)


def rotate_to_source(stacked, me, count):
    order = (me - jnp.arange(count)) % count
    return jnp.take(stacked, order, axis=0)


def local(residual, spec_gain, factor_panel, diag_inverse):
    nf = lax.axis_size("freq")
    ns = lax.axis_size("sens")
    fi = lax.axis_index("freq")
    si = lax.axis_index("sens")
    pos = si * nf + fi
    block = factor_panel.shape[0]
    tl = residual.shape[1]
    n = tl * nf
    head = STEPS * block
    f32, bf16 = jnp.float32, jnp.bfloat16

    taps = jnp.fft.irfft(spec_gain, n=n).astype(f32)
    kernel = circulant(taps)

    own = lax.all_to_all(residual, "freq", split_axis=0, concat_axis=1, tiled=True)
    field = jnp.dot(own, kernel, preferred_element_type=f32)

    piece = block // nf
    cols = (STEPS - 1) * block
    got = []
    for d in range(1, nf):
        start = ((fi + d) % nf) * piece
        mine = lax.dynamic_slice_in_dim(factor_panel, start, piece, axis=0)[:, :cols]
        pairs = [(src, (src + d) % nf) for src in range(1, STEPS)]
        got.append(lax.ppermute(mine, ALL, pairs))
    own_piece = lax.dynamic_slice_in_dim(factor_panel, fi * piece, piece, axis=0)[:, :cols]
    part1 = jnp.where(fi == 1, own_piece, 0).astype(bf16)
    part2 = jnp.where(fi == 2, own_piece, 0).astype(bf16)
    for d in range(1, nf):
        part1 = part1 + jnp.where(fi == (1 + d) % nf, got[d - 1], 0).astype(bf16)
        part2 = part2 + jnp.where(fi == (2 + d) % nf, got[d - 1], 0).astype(bf16)
    mixed = jnp.concatenate([part1[:, :block], part2], axis=1)
    stacked = [mixed]
    for d in range(1, nf):
        pairs = [(j, (j + d) % nf) for j in range(nf)]
        stacked.append(lax.ppermute(mixed, ALL, pairs))
    panels = rotate_to_source(jnp.stack(stacked), fi, nf).reshape(nf * piece, STEPS * block)
    p10 = panels[:, :block]
    p20 = panels[:, block : 2 * block]
    p21 = panels[:, 2 * block :]

    rows = [residual[k * block : (k + 1) * block] for k in range(STEPS)]
    inv = [diag_inverse[k * block : (k + 1) * block] for k in range(STEPS)]
    y0 = jnp.dot(inv[0], rows[0], preferred_element_type=f32).astype(bf16)
    z1 = rows[1].astype(f32) - jnp.dot(p10, y0, preferred_element_type=f32)
    y1 = jnp.dot(inv[1], z1.astype(bf16), preferred_element_type=f32).astype(bf16)
    z2 = (
        rows[2].astype(f32)
        - jnp.dot(p20, y0, preferred_element_type=f32)
        - jnp.dot(p21, y1, preferred_element_type=f32)
    )
    y2 = jnp.dot(inv[2], z2.astype(bf16), preferred_element_type=f32).astype(bf16)
    ys = jnp.concatenate([y0, y1, y2], axis=0)

    rs = head // ns
    mine = ys[:rs]
    for s in range(1, ns):
        recv = lax.ppermute(ys[s * rs : (s + 1) * rs], ALL, [(f, s * nf + f) for f in range(nf)])
        mine = jnp.where(si == s, recv, mine)
    yrows = lax.all_gather(mine, "freq", axis=0, tiled=False)
    yrows = jnp.transpose(yrows, (1, 0, 2)).reshape(rs, n)
    srows = jnp.dot(yrows, kernel, preferred_element_type=f32).astype(bf16)
    solved = lax.all_gather(srows, "sens", axis=0, tiled=True)

    update = jnp.dot(factor_panel, solved, preferred_element_type=f32)
    rest = (field - update).astype(bf16)
    step_rows = lax.dynamic_slice_in_dim(solved, jnp.minimum(pos, STEPS - 1) * block, block, axis=0)
    return jnp.where(pos < STEPS, step_rows, rest)


def solution(mesh):
    in_specs = (P("sens", "freq"), P(), P(("sens", "freq"), None), P())
    out_specs = P(("sens", "freq"), None)
    return jax.shard_map(local, mesh=mesh, in_specs=in_specs, out_specs=out_specs, check_vma=False)
```

```python
import jax
import jax.numpy as jnp
from jax import lax
from jax.sharding import PartitionSpec as P

STEPS = 3
ALL = ("sens", "freq")


def circulant(taps):
    n = taps.shape[0]
    nb = 128
    row = lax.broadcasted_iota(jnp.int32, (nb, n), 0)
    band = jnp.broadcast_to(taps[None, :], (nb, n))
    for bit in range(7):
        band = jnp.where(((row >> bit) & 1) == 1, jnp.roll(band, 1 << bit, axis=1), band)
    band = band.astype(jnp.bfloat16)
    return jnp.concatenate([jnp.roll(band, nb * a, axis=1) for a in range(n // nb)], axis=0)


def rotate_to_source(stacked, me, count):
    doubled = jnp.concatenate([stacked[::-1], stacked[::-1]], axis=0)
    return lax.dynamic_slice_in_dim(doubled, count - 1 - me, count, axis=0)


def local(residual, spec_gain, factor_panel, diag_inverse):
    nf = lax.axis_size("freq")
    ns = lax.axis_size("sens")
    fi = lax.axis_index("freq")
    si = lax.axis_index("sens")
    pos = si * nf + fi
    block = factor_panel.shape[0]
    tl = residual.shape[1]
    n = tl * nf
    head = STEPS * block
    f32, bf16 = jnp.float32, jnp.bfloat16

    taps = jnp.fft.irfft(spec_gain, n=n).astype(f32)
    kernel = circulant(taps)

    own = lax.all_to_all(residual, "freq", split_axis=0, concat_axis=1, tiled=True)
    field = jnp.dot(own, kernel, preferred_element_type=f32)

    piece = block // nf
    cols = (STEPS - 1) * block
    got = []
    for d in range(1, nf):
        start = ((fi + d) % nf) * piece
        mine = lax.dynamic_slice_in_dim(factor_panel, start, piece, axis=0)[:, :cols]
        pairs = [(src, (src + d) % nf) for src in range(1, STEPS)]
        got.append(lax.ppermute(mine, ALL, pairs))
    own_piece = lax.dynamic_slice_in_dim(factor_panel, fi * piece, piece, axis=0)[:, :cols]
    part1 = jnp.where(fi == 1, own_piece, 0).astype(bf16)
    part2 = jnp.where(fi == 2, own_piece, 0).astype(bf16)
    for d in range(1, nf):
        part1 = part1 + jnp.where(fi == (1 + d) % nf, got[d - 1], 0).astype(bf16)
        part2 = part2 + jnp.where(fi == (2 + d) % nf, got[d - 1], 0).astype(bf16)
    mixed = jnp.concatenate([part1[:, :block], part2], axis=1)
    stacked = [mixed]
    for d in range(1, nf):
        pairs = [(j, (j + d) % nf) for j in range(nf)]
        stacked.append(lax.ppermute(mixed, ALL, pairs))
    panels = rotate_to_source(jnp.stack(stacked), fi, nf).reshape(nf * piece, STEPS * block)
    p10 = panels[:, :block]
    p20 = panels[:, block : 2 * block]
    p21 = panels[:, 2 * block :]

    rows = [residual[k * block : (k + 1) * block] for k in range(STEPS)]
    inv = [diag_inverse[k * block : (k + 1) * block] for k in range(STEPS)]
    y0 = jnp.dot(inv[0], rows[0], preferred_element_type=f32).astype(bf16)
    z1 = rows[1].astype(f32) - jnp.dot(p10, y0, preferred_element_type=f32)
    y1 = jnp.dot(inv[1], z1.astype(bf16), preferred_element_type=f32).astype(bf16)
    z2 = (
        rows[2].astype(f32)
        - jnp.dot(p20, y0, preferred_element_type=f32)
        - jnp.dot(p21, y1, preferred_element_type=f32)
    )
    y2 = jnp.dot(inv[2], z2.astype(bf16), preferred_element_type=f32).astype(bf16)
    ys = jnp.concatenate([y0, y1, y2], axis=0)

    rs = head // ns
    mine = ys[:rs]
    for s in range(1, ns):
        recv = lax.ppermute(ys[s * rs : (s + 1) * rs], ALL, [(f, s * nf + f) for f in range(nf)])
        mine = jnp.where(si == s, recv, mine)
    got = [mine]
    for d in range(1, nf):
        got.append(lax.ppermute(mine, ALL, [(s * nf + f, s * nf + (f + d) % nf) for s in range(ns) for f in range(nf)]))
    yrows = rotate_to_source(jnp.stack(got), fi, nf)
    yrows = jnp.transpose(yrows, (1, 0, 2)).reshape(rs, n)
    srows = jnp.dot(yrows, kernel, preferred_element_type=f32).astype(bf16)
    solved = lax.all_gather(srows, "sens", axis=0, tiled=True)

    update = jnp.dot(factor_panel, solved, preferred_element_type=f32)
    rest = (field - update).astype(bf16)
    step_rows = lax.dynamic_slice_in_dim(solved, jnp.minimum(pos, STEPS - 1) * block, block, axis=0)
    return jnp.where(pos < STEPS, step_rows, rest)


def solution(mesh):
    in_specs = (P("sens", "freq"), P(), P(("sens", "freq"), None), P())
    out_specs = P(("sens", "freq"), None)
    return jax.shard_map(local, mesh=mesh, in_specs=in_specs, out_specs=out_specs, check_vma=False)
```

```python
import jax
import jax.numpy as jnp
from jax import lax
from jax.sharding import PartitionSpec as P

STEPS = 3
ALL = ("sens", "freq")


def circulant(taps):
    n = taps.shape[0]
    nb = 128
    row = lax.broadcasted_iota(jnp.int32, (nb, n), 0)
    band = jnp.broadcast_to(taps[None, :], (nb, n))
    for bit in range(7):
        band = jnp.where(((row >> bit) & 1) == 1, jnp.roll(band, 1 << bit, axis=1), band)
    band = band.astype(jnp.bfloat16)
    return jnp.concatenate([jnp.roll(band, nb * a, axis=1) for a in range(n // nb)], axis=0)


def rotate_to_source(stacked, me, count):
    doubled = jnp.concatenate([stacked, stacked], axis=0)
    return lax.dynamic_slice_in_dim(doubled, count - me, count, axis=0)


def local(residual, spec_gain, factor_panel, diag_inverse):
    nf = lax.axis_size("freq")
    ns = lax.axis_size("sens")
    fi = lax.axis_index("freq")
    si = lax.axis_index("sens")
    pos = si * nf + fi
    block = factor_panel.shape[0]
    tl = residual.shape[1]
    n = tl * nf
    head = STEPS * block
    f32, bf16 = jnp.float32, jnp.bfloat16

    taps = jnp.fft.irfft(spec_gain, n=n).astype(f32)
    kernel = circulant(taps)

    own = lax.all_to_all(residual, "freq", split_axis=0, concat_axis=1, tiled=True)
    field = jnp.dot(own, kernel, preferred_element_type=f32)

    piece = block // nf
    cols = (STEPS - 1) * block
    got = []
    for d in range(1, nf):
        start = ((fi + d) % nf) * piece
        mine = lax.dynamic_slice_in_dim(factor_panel, start, piece, axis=0)[:, :cols]
        pairs = [(src, (src + d) % nf) for src in range(1, STEPS)]
        got.append(lax.ppermute(mine, ALL, pairs))
    own_piece = lax.dynamic_slice_in_dim(factor_panel, fi * piece, piece, axis=0)[:, :cols]
    part1 = jnp.where(fi == 1, own_piece, 0).astype(bf16)
    part2 = jnp.where(fi == 2, own_piece, 0).astype(bf16)
    for d in range(1, nf):
        part1 = part1 + jnp.where(fi == (1 + d) % nf, got[d - 1], 0).astype(bf16)
        part2 = part2 + jnp.where(fi == (2 + d) % nf, got[d - 1], 0).astype(bf16)
    mixed = jnp.concatenate([part1[:, :block], part2], axis=1)
    stacked = [mixed]
    for d in range(1, nf):
        pairs = [(j, (j - d) % nf) for j in range(nf)]
        stacked.append(lax.ppermute(mixed, ALL, pairs))
    panels = rotate_to_source(jnp.stack(stacked), fi, nf).reshape(nf * piece, STEPS * block)
    p10 = panels[:, :block]
    p20 = panels[:, block : 2 * block]
    p21 = panels[:, 2 * block :]

    own, headrows = lax.optimization_barrier((own, residual[:head]))
    rows = [headrows[k * block : (k + 1) * block] for k in range(STEPS)]
    inv = [diag_inverse[k * block : (k + 1) * block] for k in range(STEPS)]
    y0 = jnp.dot(inv[0], rows[0], preferred_element_type=f32).astype(bf16)
    z1 = rows[1].astype(f32) - jnp.dot(p10, y0, preferred_element_type=f32)
    y1 = jnp.dot(inv[1], z1.astype(bf16), preferred_element_type=f32).astype(bf16)
    z2 = (
        rows[2].astype(f32)
        - jnp.dot(p20, y0, preferred_element_type=f32)
        - jnp.dot(p21, y1, preferred_element_type=f32)
    )
    y2 = jnp.dot(inv[2], z2.astype(bf16), preferred_element_type=f32).astype(bf16)
    ys = jnp.concatenate([y0, y1, y2], axis=0)

    rs = head // ns
    spread = lax.all_to_all(ys.reshape(ns, rs, tl), "sens", 0, 0, tiled=False)
    mine = spread[0]
    copies = jnp.broadcast_to(mine[None], (nf, rs, tl))
    yrows = lax.all_to_all(copies, "freq", 0, 0, tiled=False)
    yrows = jnp.transpose(yrows, (1, 0, 2)).reshape(rs, n)
    srows = jnp.dot(yrows, kernel, preferred_element_type=f32).astype(bf16)
    solved = lax.all_gather(srows, "sens", axis=0, tiled=True)

    update = jnp.dot(factor_panel, solved, preferred_element_type=f32)
    rest = (field - update).astype(bf16)
    step_rows = lax.dynamic_slice_in_dim(solved, jnp.minimum(pos, STEPS - 1) * block, block, axis=0)
    return jnp.where(pos < STEPS, step_rows, rest)


def solution(mesh):
    in_specs = (P("sens", "freq"), P(), P(("sens", "freq"), None), P())
    out_specs = P(("sens", "freq"), None)
    return jax.shard_map(local, mesh=mesh, in_specs=in_specs, out_specs=out_specs, check_vma=False)
```

```python
import jax
import jax.numpy as jnp
from jax import lax
from jax.sharding import PartitionSpec as P

STEPS = 3
ALL = ("sens", "freq")


def circulant(taps):
    n = taps.shape[0]
    nb = 128
    row = lax.broadcasted_iota(jnp.int32, (nb, n), 0)
    band = jnp.broadcast_to(taps[None, :], (nb, n))
    for bit in range(7):
        band = jnp.where(((row >> bit) & 1) == 1, jnp.roll(band, 1 << bit, axis=1), band)
    band = band.astype(jnp.bfloat16)
    return jnp.concatenate([jnp.roll(band, nb * a, axis=1) for a in range(n // nb)], axis=0)


def rotate_to_source(stacked, me, count):
    doubled = jnp.concatenate([stacked, stacked], axis=0)
    return lax.dynamic_slice_in_dim(doubled, count - me, count, axis=0)


def local(residual, spec_gain, factor_panel, diag_inverse):
    nf = lax.axis_size("freq")
    ns = lax.axis_size("sens")
    fi = lax.axis_index("freq")
    si = lax.axis_index("sens")
    pos = si * nf + fi
    block = factor_panel.shape[0]
    tl = residual.shape[1]
    n = tl * nf
    head = STEPS * block
    f32, bf16 = jnp.float32, jnp.bfloat16

    taps = jnp.fft.irfft(spec_gain, n=n).astype(f32)
    kernel = circulant(taps)

    own = lax.all_to_all(residual, "freq", split_axis=0, concat_axis=1, tiled=True)
    field = jnp.dot(own, kernel, preferred_element_type=f32)

    piece = block // nf
    cols = (STEPS - 1) * block
    got = []
    for d in range(1, nf):
        start = ((fi + d) % nf) * piece
        mine = lax.dynamic_slice_in_dim(factor_panel, start, piece, axis=0)[:, :cols]
        pairs = [(src, (src + d) % nf) for src in range(1, STEPS)]
        got.append(lax.ppermute(mine, ALL, pairs))
    own_piece = lax.dynamic_slice_in_dim(factor_panel, fi * piece, piece, axis=0)[:, :cols]
    part1 = jnp.where(fi == 1, own_piece, 0).astype(bf16)
    part2 = jnp.where(fi == 2, own_piece, 0).astype(bf16)
    for d in range(1, nf):
        part1 = part1 + jnp.where(fi == (1 + d) % nf, got[d - 1], 0).astype(bf16)
        part2 = part2 + jnp.where(fi == (2 + d) % nf, got[d - 1], 0).astype(bf16)
    mixed = jnp.concatenate([part1[:, :block], part2], axis=1)
    stacked = [mixed]
    for d in range(1, nf):
        pairs = [(j, (j - d) % nf) for j in range(nf)]
        stacked.append(lax.ppermute(mixed, ALL, pairs))
    panels = rotate_to_source(jnp.stack(stacked), fi, nf).reshape(nf * piece, STEPS * block)
    p10 = panels[:, :block]
    p20 = panels[:, block : 2 * block]
    p21 = panels[:, 2 * block :]

    inv = [diag_inverse[k * block : (k + 1) * block] for k in range(STEPS)]
    y0 = jnp.dot(inv[0], residual[:block], preferred_element_type=f32).astype(bf16)
    solved0 = spread_and_filter(y0, kernel, ns, nf)
    own, headrows = lax.optimization_barrier((own, residual[:head]))
    rows = [headrows[k * block : (k + 1) * block] for k in range(STEPS)]
    z1 = rows[1].astype(f32) - jnp.dot(p10, y0, preferred_element_type=f32)
    y1 = jnp.dot(inv[1], z1.astype(bf16), preferred_element_type=f32).astype(bf16)
    z2 = (
        rows[2].astype(f32)
        - jnp.dot(p20, y0, preferred_element_type=f32)
        - jnp.dot(p21, y1, preferred_element_type=f32)
    )
    y2 = jnp.dot(inv[2], z2.astype(bf16), preferred_element_type=f32).astype(bf16)
    solved12 = spread_and_filter(jnp.concatenate([y1, y2], axis=0), kernel, ns, nf)

    update = jnp.dot(factor_panel[:, :block], solved0, preferred_element_type=f32)
    update = update + jnp.dot(factor_panel[:, block:], solved12, preferred_element_type=f32)
    rest = (field - update).astype(bf16)
    first = jnp.where(pos == 1, solved12[:block], solved0)
    step_rows = jnp.where(pos == 2, solved12[block:], first)
    return jnp.where(pos < STEPS, step_rows, rest)


def spread_and_filter(ys, kernel, ns, nf):
    rows, tl = ys.shape
    rs = rows // ns
    spread = lax.all_to_all(ys.reshape(ns, rs, tl), "sens", 0, 0, tiled=False)
    copies = jnp.broadcast_to(spread[0][None], (nf, rs, tl))
    yrows = lax.all_to_all(copies, "freq", 0, 0, tiled=False)
    yrows = jnp.transpose(yrows, (1, 0, 2)).reshape(rs, nf * tl)
    srows = jnp.dot(yrows, kernel, preferred_element_type=jnp.float32).astype(jnp.bfloat16)
    return lax.all_gather(srows, "sens", axis=0, tiled=True)


def solution(mesh):
    in_specs = (P("sens", "freq"), P(), P(("sens", "freq"), None), P())
    out_specs = P(("sens", "freq"), None)
    return jax.shard_map(local, mesh=mesh, in_specs=in_specs, out_specs=out_specs, check_vma=False)
```

```python
import jax
import jax.numpy as jnp
from jax import lax
from jax.sharding import PartitionSpec as P

STEPS = 3
ALL = ("sens", "freq")


def circulant(taps):
    n = taps.shape[0]
    nb = 128
    row = lax.broadcasted_iota(jnp.int32, (nb, n), 0)
    band = jnp.broadcast_to(taps[None, :], (nb, n))
    for bit in range(7):
        band = jnp.where(((row >> bit) & 1) == 1, jnp.roll(band, 1 << bit, axis=1), band)
    band = band.astype(jnp.bfloat16)
    return jnp.concatenate([jnp.roll(band, nb * a, axis=1) for a in range(n // nb)], axis=0)


def rotate_to_source(stacked, me, count):
    doubled = jnp.concatenate([stacked, stacked], axis=0)
    return lax.dynamic_slice_in_dim(doubled, count - me, count, axis=0)


def local(residual, spec_gain, factor_panel, diag_inverse):
    nf = lax.axis_size("freq")
    ns = lax.axis_size("sens")
    fi = lax.axis_index("freq")
    si = lax.axis_index("sens")
    pos = si * nf + fi
    block = factor_panel.shape[0]
    tl = residual.shape[1]
    n = tl * nf
    head = STEPS * block
    f32, bf16 = jnp.float32, jnp.bfloat16

    taps = jnp.fft.irfft(spec_gain, n=n).astype(f32)
    kernel = circulant(taps)

    piece = block // nf
    cols = (STEPS - 1) * block
    got = []
    for d in range(1, nf):
        start = ((fi + d) % nf) * piece
        mine = lax.dynamic_slice_in_dim(factor_panel, start, piece, axis=0)[:, :cols]
        pairs = [(src, (src + d) % nf) for src in range(1, STEPS)]
        got.append(lax.ppermute(mine, ALL, pairs))
    own_piece = lax.dynamic_slice_in_dim(factor_panel, fi * piece, piece, axis=0)[:, :cols]
    part1 = jnp.where(fi == 1, own_piece, 0).astype(bf16)
    part2 = jnp.where(fi == 2, own_piece, 0).astype(bf16)
    for d in range(1, nf):
        part1 = part1 + jnp.where(fi == (1 + d) % nf, got[d - 1], 0).astype(bf16)
        part2 = part2 + jnp.where(fi == (2 + d) % nf, got[d - 1], 0).astype(bf16)
    mixed = jnp.concatenate([part1[:, :block], part2], axis=1)
    stacked = [mixed]
    for d in range(1, nf):
        pairs = [(j, (j - d) % nf) for j in range(nf)]
        stacked.append(lax.ppermute(mixed, ALL, pairs))
    panels = rotate_to_source(jnp.stack(stacked), fi, nf).reshape(nf * piece, STEPS * block)
    later, panels = lax.optimization_barrier((residual, panels))
    own = lax.all_to_all(later, "freq", split_axis=0, concat_axis=1, tiled=True)
    field = jnp.dot(own, kernel, preferred_element_type=f32)
    p10 = panels[:, :block]
    p20 = panels[:, block : 2 * block]
    p21 = panels[:, 2 * block :]

    inv = [diag_inverse[k * block : (k + 1) * block] for k in range(STEPS)]
    y0 = jnp.dot(inv[0], residual[:block], preferred_element_type=f32).astype(bf16)
    solved0 = spread_and_filter(y0, kernel, ns, nf)
    rows = [residual[k * block : (k + 1) * block] for k in range(STEPS)]
    z1 = rows[1].astype(f32) - jnp.dot(p10, y0, preferred_element_type=f32)
    y1 = jnp.dot(inv[1], z1.astype(bf16), preferred_element_type=f32).astype(bf16)
    z2 = (
        rows[2].astype(f32)
        - jnp.dot(p20, y0, preferred_element_type=f32)
        - jnp.dot(p21, y1, preferred_element_type=f32)
    )
    y2 = jnp.dot(inv[2], z2.astype(bf16), preferred_element_type=f32).astype(bf16)
    solved12 = spread_and_filter(jnp.concatenate([y1, y2], axis=0), kernel, ns, nf)

    update = jnp.dot(factor_panel[:, :block], solved0, preferred_element_type=f32)
    update = update + jnp.dot(factor_panel[:, block:], solved12, preferred_element_type=f32)
    rest = (field - update).astype(bf16)
    first = jnp.where(pos == 1, solved12[:block], solved0)
    step_rows = jnp.where(pos == 2, solved12[block:], first)
    return jnp.where(pos < STEPS, step_rows, rest)


def spread_and_filter(ys, kernel, ns, nf):
    rows, tl = ys.shape
    rs = rows // ns
    spread = lax.all_to_all(ys.reshape(ns, rs, tl), "sens", 0, 0, tiled=False)
    copies = jnp.broadcast_to(spread[0][None], (nf, rs, tl))
    yrows = lax.all_to_all(copies, "freq", 0, 0, tiled=False)
    yrows = jnp.transpose(yrows, (1, 0, 2)).reshape(rs, nf * tl)
    srows = jnp.dot(yrows, kernel, preferred_element_type=jnp.float32).astype(jnp.bfloat16)
    return lax.all_gather(srows, "sens", axis=0, tiled=True)


def solution(mesh):
    in_specs = (P("sens", "freq"), P(), P(("sens", "freq"), None), P())
    out_specs = P(("sens", "freq"), None)
    return jax.shard_map(local, mesh=mesh, in_specs=in_specs, out_specs=out_specs, check_vma=False)
```

```python
import jax
import jax.numpy as jnp
from jax import lax
from jax.sharding import PartitionSpec as P

STEPS = 3
ALL = ("sens", "freq")


def circulant(taps):
    n = taps.shape[0]
    nb = 128
    row = lax.broadcasted_iota(jnp.int32, (nb, n), 0)
    band = jnp.broadcast_to(taps[None, :], (nb, n))
    for bit in range(7):
        band = jnp.where(((row >> bit) & 1) == 1, jnp.roll(band, 1 << bit, axis=1), band)
    band = band.astype(jnp.bfloat16)
    return jnp.concatenate([jnp.roll(band, nb * a, axis=1) for a in range(n // nb)], axis=0)


def rotate_to_source(stacked, me, count):
    doubled = jnp.concatenate([stacked, stacked], axis=0)
    return lax.dynamic_slice_in_dim(doubled, count - me, count, axis=0)


def local(residual, spec_gain, factor_panel, diag_inverse):
    nf = lax.axis_size("freq")
    ns = lax.axis_size("sens")
    fi = lax.axis_index("freq")
    si = lax.axis_index("sens")
    pos = si * nf + fi
    block = factor_panel.shape[0]
    tl = residual.shape[1]
    n = tl * nf
    head = STEPS * block
    f32, bf16 = jnp.float32, jnp.bfloat16

    taps = jnp.fft.irfft(spec_gain, n=n).astype(f32)
    kernel = circulant(taps)

    own = lax.all_to_all(residual, "freq", split_axis=0, concat_axis=1, tiled=True)
    field = jnp.dot(own, kernel, preferred_element_type=f32)

    piece = block // nf
    cols = (STEPS - 1) * block
    got = []
    for d in range(1, nf):
        start = ((fi + d) % nf) * piece
        mine = lax.dynamic_slice_in_dim(factor_panel, start, piece, axis=0)[:, :cols]
        pairs = [(src, (src + d) % nf) for src in range(1, STEPS)]
        got.append(lax.ppermute(mine, ALL, pairs))
    own_piece = lax.dynamic_slice_in_dim(factor_panel, fi * piece, piece, axis=0)[:, :cols]
    part1 = jnp.where(fi == 1, own_piece, 0).astype(bf16)
    part2 = jnp.where(fi == 2, own_piece, 0).astype(bf16)
    for d in range(1, nf):
        part1 = part1 + jnp.where(fi == (1 + d) % nf, got[d - 1], 0).astype(bf16)
        part2 = part2 + jnp.where(fi == (2 + d) % nf, got[d - 1], 0).astype(bf16)
    mixed = jnp.concatenate([part1[:, :block], part2], axis=1)
    stacked = [mixed]
    for d in range(1, nf):
        pairs = [(j, (j - d) % nf) for j in range(nf)]
        stacked.append(lax.ppermute(mixed, ALL, pairs))
    panels = rotate_to_source(jnp.stack(stacked), fi, nf).reshape(nf * piece, STEPS * block)
    p10 = panels[:, :block]
    p20 = panels[:, block : 2 * block]
    p21 = panels[:, 2 * block :]

    own, headrows = lax.optimization_barrier((own, residual[:head]))
    rows = [headrows[k * block : (k + 1) * block] for k in range(STEPS)]
    inv = [diag_inverse[k * block : (k + 1) * block] for k in range(STEPS)]
    y0 = jnp.dot(inv[0], rows[0], preferred_element_type=f32).astype(bf16)
    z1 = rows[1].astype(f32) - jnp.dot(p10, y0, preferred_element_type=f32)
    y1 = jnp.dot(inv[1], z1.astype(bf16), preferred_element_type=f32).astype(bf16)
    z2 = (
        rows[2].astype(f32)
        - jnp.dot(p20, y0, preferred_element_type=f32)
        - jnp.dot(p21, y1, preferred_element_type=f32)
    )
    y2 = jnp.dot(inv[2], z2.astype(bf16), preferred_element_type=f32).astype(bf16)
    ys = jnp.concatenate([y0, y1, y2], axis=0)

    rs = head // ns
    spread = lax.all_to_all(ys.reshape(ns, rs, tl), "sens", 0, 0, tiled=False)
    mine = spread[0]
    copies = jnp.broadcast_to(mine[None], (nf, rs, tl))
    yrows = lax.all_to_all(copies, "freq", 0, 0, tiled=False)
    yrows = jnp.transpose(yrows, (1, 0, 2)).reshape(rs, n)
    srows = jnp.dot(yrows, kernel, preferred_element_type=f32).astype(bf16)
    half = rs // 2
    parts = [lax.all_gather(srows[h * half : (h + 1) * half], "sens", axis=0, tiled=False) for h in range(2)]
    solved = jnp.stack(parts, axis=1).reshape(head, n)
    pan = factor_panel.reshape(block, ns, 2, half)
    update = jnp.dot(pan[:, :, 0, :].reshape(block, ns * half), parts[0].reshape(ns * half, n), preferred_element_type=f32)
    update = update + jnp.dot(pan[:, :, 1, :].reshape(block, ns * half), parts[1].reshape(ns * half, n), preferred_element_type=f32)
    rest = (field - update).astype(bf16)
    step_rows = lax.dynamic_slice_in_dim(solved, jnp.minimum(pos, STEPS - 1) * block, block, axis=0)
    return jnp.where(pos < STEPS, step_rows, rest)


def solution(mesh):
    in_specs = (P("sens", "freq"), P(), P(("sens", "freq"), None), P())
    out_specs = P(("sens", "freq"), None)
    return jax.shard_map(local, mesh=mesh, in_specs=in_specs, out_specs=out_specs, check_vma=False)
```

```python
import jax
import jax.numpy as jnp
from jax import lax
from jax.sharding import PartitionSpec as P

STEPS = 3
ALL = ("sens", "freq")


def circulant(taps):
    n = taps.shape[0]
    nb = 128
    row = lax.broadcasted_iota(jnp.int32, (nb, n), 0)
    band = jnp.broadcast_to(taps[None, :], (nb, n))
    for bit in range(7):
        band = jnp.where(((row >> bit) & 1) == 1, jnp.roll(band, 1 << bit, axis=1), band)
    band = band.astype(jnp.bfloat16)
    return jnp.concatenate([jnp.roll(band, nb * a, axis=1) for a in range(n // nb)], axis=0)


def rotate_to_source(stacked, me, count):
    doubled = jnp.concatenate([stacked[::-1], stacked[::-1]], axis=0)
    return lax.dynamic_slice_in_dim(doubled, count - 1 - me, count, axis=0)


def local(residual, spec_gain, factor_panel, diag_inverse):
    nf = lax.axis_size("freq")
    ns = lax.axis_size("sens")
    fi = lax.axis_index("freq")
    si = lax.axis_index("sens")
    pos = si * nf + fi
    block = factor_panel.shape[0]
    tl = residual.shape[1]
    n = tl * nf
    head = STEPS * block
    f32, bf16 = jnp.float32, jnp.bfloat16

    taps = jnp.fft.irfft(spec_gain, n=n).astype(f32)
    kernel = circulant(taps)

    piece = block // nf
    cols = (STEPS - 1) * block
    got = []
    for d in range(1, nf):
        start = ((fi + d) % nf) * piece
        mine = lax.dynamic_slice_in_dim(factor_panel, start, piece, axis=0)[:, :cols]
        pairs = [(src, (src + d) % nf) for src in range(1, STEPS)]
        got.append(lax.ppermute(mine, ALL, pairs))
    own_piece = lax.dynamic_slice_in_dim(factor_panel, fi * piece, piece, axis=0)[:, :cols]
    part1 = jnp.where(fi == 1, own_piece, 0).astype(bf16)
    part2 = jnp.where(fi == 2, own_piece, 0).astype(bf16)
    for d in range(1, nf):
        part1 = part1 + jnp.where(fi == (1 + d) % nf, got[d - 1], 0).astype(bf16)
        part2 = part2 + jnp.where(fi == (2 + d) % nf, got[d - 1], 0).astype(bf16)
    mixed = jnp.concatenate([part1[:, :block], part2], axis=1)
    stacked = [mixed]
    for d in range(1, nf):
        pairs = [(j, (j + d) % nf) for j in range(nf)]
        stacked.append(lax.ppermute(mixed, ALL, pairs))
    panels = rotate_to_source(jnp.stack(stacked), fi, nf).reshape(nf * piece, STEPS * block)
    later, panels = lax.optimization_barrier((residual, panels))
    own = lax.all_to_all(later, "freq", split_axis=0, concat_axis=1, tiled=True)
    p10 = panels[:, :block]
    p20 = panels[:, block : 2 * block]
    p21 = panels[:, 2 * block :]

    rows = [residual[k * block : (k + 1) * block] for k in range(STEPS)]
    inv = [diag_inverse[k * block : (k + 1) * block] for k in range(STEPS)]
    y0 = jnp.dot(inv[0], rows[0], preferred_element_type=f32).astype(bf16)
    z1 = rows[1].astype(f32) - jnp.dot(p10, y0, preferred_element_type=f32)
    y1 = jnp.dot(inv[1], z1.astype(bf16), preferred_element_type=f32).astype(bf16)
    z2 = (
        rows[2].astype(f32)
        - jnp.dot(p20, y0, preferred_element_type=f32)
        - jnp.dot(p21, y1, preferred_element_type=f32)
    )
    y2 = jnp.dot(inv[2], z2.astype(bf16), preferred_element_type=f32).astype(bf16)
    ys = jnp.concatenate([y0, y1, y2], axis=0)

    rs = head // ns
    mine = ys[:rs]
    for s in range(1, ns):
        recv = lax.ppermute(ys[s * rs : (s + 1) * rs], ALL, [(f, s * nf + f) for f in range(nf)])
        mine = jnp.where(si == s, recv, mine)
    got = [mine]
    for d in range(1, nf):
        got.append(lax.ppermute(mine, ALL, [(s * nf + f, s * nf + (f + d) % nf) for s in range(ns) for f in range(nf)]))
    yrows = rotate_to_source(jnp.stack(got), fi, nf)
    yrows = jnp.transpose(yrows, (1, 0, 2)).reshape(rs, n)
    srows = jnp.dot(yrows, kernel, preferred_element_type=f32).astype(bf16)
    field = jnp.dot(own, kernel, preferred_element_type=f32)
    field, srows = lax.optimization_barrier((field, srows))
    solved = lax.all_gather(srows, "sens", axis=0, tiled=True)

    update = jnp.dot(factor_panel, solved, preferred_element_type=f32)
    rest = (field - update).astype(bf16)
    step_rows = lax.dynamic_slice_in_dim(solved, jnp.minimum(pos, STEPS - 1) * block, block, axis=0)
    return jnp.where(pos < STEPS, step_rows, rest)


def solution(mesh):
    in_specs = (P("sens", "freq"), P(), P(("sens", "freq"), None), P())
    out_specs = P(("sens", "freq"), None)
    return jax.shard_map(local, mesh=mesh, in_specs=in_specs, out_specs=out_specs, check_vma=False)
```

```python
import jax
import jax.numpy as jnp
from jax import lax
from jax.sharding import PartitionSpec as P

STEPS = 3
ALL = ("sens", "freq")


def circulant(taps):
    n = taps.shape[0]
    nb = 128
    row = lax.broadcasted_iota(jnp.int32, (nb, n), 0)
    band = jnp.broadcast_to(taps[None, :], (nb, n))
    for bit in range(7):
        band = jnp.where(((row >> bit) & 1) == 1, jnp.roll(band, 1 << bit, axis=1), band)
    band = band.astype(jnp.bfloat16)
    return jnp.concatenate([jnp.roll(band, nb * a, axis=1) for a in range(n // nb)], axis=0)


def split(x):
    hi = x.astype(jnp.bfloat16)
    return hi, (x - hi.astype(jnp.float32)).astype(jnp.bfloat16)


def dot_left(a, x):
    hi, lo = split(x)
    f32 = jnp.float32
    return jnp.dot(a, hi, preferred_element_type=f32) + jnp.dot(a, lo, preferred_element_type=f32)


def dot_right(x, b):
    hi, lo = split(x)
    f32 = jnp.float32
    return jnp.dot(hi, b, preferred_element_type=f32) + jnp.dot(lo, b, preferred_element_type=f32)


def rotate_to_source(stacked, me, count):
    doubled = jnp.concatenate([stacked, stacked], axis=0)
    return lax.dynamic_slice_in_dim(doubled, count - me, count, axis=0)


def local(residual, spec_gain, factor_panel, diag_inverse):
    nf = lax.axis_size("freq")
    ns = lax.axis_size("sens")
    fi = lax.axis_index("freq")
    si = lax.axis_index("sens")
    pos = si * nf + fi
    block = factor_panel.shape[0]
    tl = residual.shape[1]
    n = tl * nf
    head = STEPS * block
    f32, bf16 = jnp.float32, jnp.bfloat16

    taps = jnp.fft.irfft(spec_gain, n=n).astype(f32)
    kernel = circulant(taps)

    own = lax.all_to_all(residual, "freq", split_axis=0, concat_axis=1, tiled=True)
    field = jnp.dot(own, kernel, preferred_element_type=f32)

    piece = block // nf
    cols = (STEPS - 1) * block
    got = []
    for d in range(1, nf):
        start = ((fi + d) % nf) * piece
        mine = lax.dynamic_slice_in_dim(factor_panel, start, piece, axis=0)[:, :cols]
        pairs = [(src, (src + d) % nf) for src in range(1, STEPS)]
        got.append(lax.ppermute(mine, ALL, pairs))
    own_piece = lax.dynamic_slice_in_dim(factor_panel, fi * piece, piece, axis=0)[:, :cols]
    part1 = jnp.where(fi == 1, own_piece, 0).astype(bf16)
    part2 = jnp.where(fi == 2, own_piece, 0).astype(bf16)
    for d in range(1, nf):
        part1 = part1 + jnp.where(fi == (1 + d) % nf, got[d - 1], 0).astype(bf16)
        part2 = part2 + jnp.where(fi == (2 + d) % nf, got[d - 1], 0).astype(bf16)
    mixed = jnp.concatenate([part1[:, :block], part2], axis=1)
    stacked = [mixed]
    for d in range(1, nf):
        pairs = [(j, (j - d) % nf) for j in range(nf)]
        stacked.append(lax.ppermute(mixed, ALL, pairs))
    panels = rotate_to_source(jnp.stack(stacked), fi, nf).reshape(nf * piece, STEPS * block)
    p10 = panels[:, :block]
    p20 = panels[:, block : 2 * block]
    p21 = panels[:, 2 * block :]

    own, headrows = lax.optimization_barrier((own, residual[:head]))
    rows = [headrows[k * block : (k + 1) * block] for k in range(STEPS)]
    inv = [diag_inverse[k * block : (k + 1) * block] for k in range(STEPS)]
    y0 = jnp.dot(inv[0], rows[0], preferred_element_type=f32)
    z1 = rows[1].astype(f32) - dot_left(p10, y0)
    y1 = dot_left(inv[1], z1)
    z2 = rows[2].astype(f32) - dot_left(p20, y0) - dot_left(p21, y1)
    y2 = dot_left(inv[2], z2)
    ys = jnp.concatenate([y0, y1, y2], axis=0)

    rs = head // ns
    spread = lax.all_to_all(ys.reshape(ns, rs, tl), "sens", 0, 0, tiled=False)
    mine = spread[0]
    copies = jnp.broadcast_to(mine[None], (nf, rs, tl))
    yrows = lax.all_to_all(copies, "freq", 0, 0, tiled=False)
    yrows = jnp.transpose(yrows, (1, 0, 2)).reshape(rs, n)
    srows = dot_right(yrows, kernel).astype(bf16)
    solved = lax.all_gather(srows, "sens", axis=0, tiled=True)

    update = jnp.dot(factor_panel, solved, preferred_element_type=f32)
    rest = (field - update).astype(bf16)
    step_rows = lax.dynamic_slice_in_dim(solved, jnp.minimum(pos, STEPS - 1) * block, block, axis=0)
    return jnp.where(pos < STEPS, step_rows, rest)


def solution(mesh):
    in_specs = (P("sens", "freq"), P(), P(("sens", "freq"), None), P())
    out_specs = P(("sens", "freq"), None)
    return jax.shard_map(local, mesh=mesh, in_specs=in_specs, out_specs=out_specs, check_vma=False)
```

```python
import jax
import jax.numpy as jnp
from jax import lax
from jax.sharding import PartitionSpec as P

STEPS = 3
ALL = ("sens", "freq")


def circulant(taps):
    n = taps.shape[0]
    nb = 128
    row = lax.broadcasted_iota(jnp.int32, (nb, n), 0)
    band = jnp.broadcast_to(taps[None, :], (nb, n))
    for bit in range(7):
        band = jnp.where(((row >> bit) & 1) == 1, jnp.roll(band, 1 << bit, axis=1), band)
    band = band.astype(jnp.bfloat16)
    return jnp.concatenate([jnp.roll(band, nb * a, axis=1) for a in range(n // nb)], axis=0)


def split(x):
    hi = x.astype(jnp.bfloat16)
    return hi, (x - hi.astype(jnp.float32)).astype(jnp.bfloat16)


def dot_left(a, x):
    hi, lo = split(x)
    f32 = jnp.float32
    return jnp.dot(a, hi, preferred_element_type=f32) + jnp.dot(a, lo, preferred_element_type=f32)


def dot_right(x, b):
    hi, lo = split(x)
    f32 = jnp.float32
    return jnp.dot(hi, b, preferred_element_type=f32) + jnp.dot(lo, b, preferred_element_type=f32)


def rotate_to_source(stacked, me, count):
    doubled = jnp.concatenate([stacked, stacked], axis=0)
    return lax.dynamic_slice_in_dim(doubled, count - me, count, axis=0)


def local(residual, spec_gain, factor_panel, diag_inverse):
    nf = lax.axis_size("freq")
    ns = lax.axis_size("sens")
    fi = lax.axis_index("freq")
    si = lax.axis_index("sens")
    pos = si * nf + fi
    block = factor_panel.shape[0]
    tl = residual.shape[1]
    n = tl * nf
    head = STEPS * block
    f32, bf16 = jnp.float32, jnp.bfloat16

    taps = jnp.fft.irfft(spec_gain, n=n).astype(f32)
    kernel = circulant(taps)

    own = lax.all_to_all(residual, "freq", split_axis=0, concat_axis=1, tiled=True)
    field = jnp.dot(own, kernel, preferred_element_type=f32)

    piece = block // nf
    cols = (STEPS - 1) * block
    got = []
    for d in range(1, nf):
        start = ((fi + d) % nf) * piece
        mine = lax.dynamic_slice_in_dim(factor_panel, start, piece, axis=0)[:, :cols]
        pairs = [(src, (src + d) % nf) for src in range(1, STEPS)]
        got.append(lax.ppermute(mine, ALL, pairs))
    own_piece = lax.dynamic_slice_in_dim(factor_panel, fi * piece, piece, axis=0)[:, :cols]
    part1 = jnp.where(fi == 1, own_piece, 0).astype(bf16)
    part2 = jnp.where(fi == 2, own_piece, 0).astype(bf16)
    for d in range(1, nf):
        part1 = part1 + jnp.where(fi == (1 + d) % nf, got[d - 1], 0).astype(bf16)
        part2 = part2 + jnp.where(fi == (2 + d) % nf, got[d - 1], 0).astype(bf16)
    mixed = jnp.concatenate([part1[:, :block], part2], axis=1)
    stacked = [mixed]
    for d in range(1, nf):
        pairs = [(j, (j - d) % nf) for j in range(nf)]
        stacked.append(lax.ppermute(mixed, ALL, pairs))
    panels = rotate_to_source(jnp.stack(stacked), fi, nf).reshape(nf * piece, STEPS * block)
    p10 = panels[:, :block]
    p20 = panels[:, block : 2 * block]
    p21 = panels[:, 2 * block :]

    own, headrows = lax.optimization_barrier((own, residual[:head]))
    rows = [headrows[k * block : (k + 1) * block] for k in range(STEPS)]
    inv = [diag_inverse[k * block : (k + 1) * block] for k in range(STEPS)]
    y0 = jnp.dot(inv[0], rows[0], preferred_element_type=f32)
    z1 = rows[1].astype(f32) - dot_left(p10, y0)
    y1 = dot_left(inv[1], z1)
    z2 = rows[2].astype(f32) - dot_left(p20, y0) - dot_left(p21, y1)
    y2 = dot_left(inv[2], z2)
    ys = jnp.concatenate([y0, y1, y2], axis=0)

    rs = head // ns
    mine = ys[:rs]
    for s in range(1, ns):
        recv = lax.ppermute(ys[s * rs : (s + 1) * rs], ALL, [(f, s * nf + f) for f in range(nf)])
        mine = jnp.where(si == s, recv, mine)
    copies = jnp.broadcast_to(mine[None], (nf, rs, tl))
    yrows = lax.all_to_all(copies, "freq", 0, 0, tiled=False)
    yrows = jnp.transpose(yrows, (1, 0, 2)).reshape(rs, n)
    srows = dot_right(yrows, kernel).astype(bf16)
    solved = lax.all_gather(srows, "sens", axis=0, tiled=True)

    update = jnp.dot(factor_panel, solved, preferred_element_type=f32)
    rest = (field - update).astype(bf16)
    step_rows = lax.dynamic_slice_in_dim(solved, jnp.minimum(pos, STEPS - 1) * block, block, axis=0)
    return jnp.where(pos < STEPS, step_rows, rest)


def solution(mesh):
    in_specs = (P("sens", "freq"), P(), P(("sens", "freq"), None), P())
    out_specs = P(("sens", "freq"), None)
    return jax.shard_map(local, mesh=mesh, in_specs=in_specs, out_specs=out_specs, check_vma=False)
```

```python
import jax
import jax.numpy as jnp
from jax import lax
from jax.sharding import PartitionSpec as P

STEPS = 3
ALL = ("sens", "freq")


def circulant(taps):
    n = taps.shape[0]
    nb = 128
    row = lax.broadcasted_iota(jnp.int32, (nb, n), 0)
    band = jnp.broadcast_to(taps[None, :], (nb, n))
    for bit in range(7):
        band = jnp.where(((row >> bit) & 1) == 1, jnp.roll(band, 1 << bit, axis=1), band)
    band = band.astype(jnp.bfloat16)
    return jnp.concatenate([jnp.roll(band, nb * a, axis=1) for a in range(n // nb)], axis=0)


def split(x):
    hi = x.astype(jnp.bfloat16)
    return hi, (x - hi.astype(jnp.float32)).astype(jnp.bfloat16)


def dot_left(a, x):
    hi, lo = split(x)
    f32 = jnp.float32
    return jnp.dot(a, hi, preferred_element_type=f32) + jnp.dot(a, lo, preferred_element_type=f32)


def dot_right(x, b):
    hi, lo = split(x)
    f32 = jnp.float32
    return jnp.dot(hi, b, preferred_element_type=f32) + jnp.dot(lo, b, preferred_element_type=f32)


def rotate_to_source(stacked, me, count):
    doubled = jnp.concatenate([stacked, stacked], axis=0)
    return lax.dynamic_slice_in_dim(doubled, count - me, count, axis=0)


def local(residual, spec_gain, factor_panel, diag_inverse):
    nf = lax.axis_size("freq")
    ns = lax.axis_size("sens")
    fi = lax.axis_index("freq")
    si = lax.axis_index("sens")
    pos = si * nf + fi
    block = factor_panel.shape[0]
    tl = residual.shape[1]
    n = tl * nf
    head = STEPS * block
    f32, bf16 = jnp.float32, jnp.bfloat16

    taps = jnp.fft.irfft(spec_gain, n=n).astype(f32)
    kernel = circulant(taps)

    own = lax.all_to_all(residual, "freq", split_axis=0, concat_axis=1, tiled=True)
    field = jnp.dot(own, kernel, preferred_element_type=f32)

    piece = block // nf
    cols = (STEPS - 1) * block
    got = []
    for d in range(1, nf):
        start = ((fi + d) % nf) * piece
        mine = lax.dynamic_slice_in_dim(factor_panel, start, piece, axis=0)[:, :cols]
        pairs = [(src, (src + d) % nf) for src in range(1, STEPS)]
        got.append(lax.ppermute(mine, ALL, pairs))
    own_piece = lax.dynamic_slice_in_dim(factor_panel, fi * piece, piece, axis=0)[:, :cols]
    part1 = jnp.where(fi == 1, own_piece, 0).astype(bf16)
    part2 = jnp.where(fi == 2, own_piece, 0).astype(bf16)
    for d in range(1, nf):
        part1 = part1 + jnp.where(fi == (1 + d) % nf, got[d - 1], 0).astype(bf16)
        part2 = part2 + jnp.where(fi == (2 + d) % nf, got[d - 1], 0).astype(bf16)
    mixed = jnp.concatenate([part1[:, :block], part2], axis=1)
    stacked = [mixed]
    for d in range(1, nf):
        pairs = [(j, (j - d) % nf) for j in range(nf)]
        stacked.append(lax.ppermute(mixed, ALL, pairs))
    panels = rotate_to_source(jnp.stack(stacked), fi, nf).reshape(nf * piece, STEPS * block)
    p10 = panels[:, :block]
    p20 = panels[:, block : 2 * block]
    p21 = panels[:, 2 * block :]

    rows = [residual[k * block : (k + 1) * block] for k in range(STEPS)]
    inv = [diag_inverse[k * block : (k + 1) * block] for k in range(STEPS)]
    y0 = jnp.dot(inv[0], rows[0], preferred_element_type=f32)
    z1 = rows[1].astype(f32) - dot_left(p10, y0)
    y1 = dot_left(inv[1], z1)
    z2 = rows[2].astype(f32) - dot_left(p20, y0) - dot_left(p21, y1)
    y2 = dot_left(inv[2], z2)
    ys = jnp.concatenate([y0, y1, y2], axis=0)

    rs = head // ns
    mine = ys[:rs]
    for s in range(1, ns):
        recv = lax.ppermute(ys[s * rs : (s + 1) * rs], ALL, [(f, s * nf + f) for f in range(nf)])
        mine = jnp.where(si == s, recv, mine)
    copies = jnp.broadcast_to(mine[None], (nf, rs, tl))
    yrows = lax.all_to_all(copies, "freq", 0, 0, tiled=False)
    yrows = jnp.transpose(yrows, (1, 0, 2)).reshape(rs, n)
    srows = dot_right(yrows, kernel).astype(bf16)
    solved = lax.all_gather(srows, "sens", axis=0, tiled=True)

    update = jnp.dot(factor_panel, solved, preferred_element_type=f32)
    rest = (field - update).astype(bf16)
    step_rows = lax.dynamic_slice_in_dim(solved, jnp.minimum(pos, STEPS - 1) * block, block, axis=0)
    return jnp.where(pos < STEPS, step_rows, rest)


def solution(mesh):
    in_specs = (P("sens", "freq"), P(), P(("sens", "freq"), None), P())
    out_specs = P(("sens", "freq"), None)
    return jax.shard_map(local, mesh=mesh, in_specs=in_specs, out_specs=out_specs, check_vma=False)
```

```python
import jax
import jax.numpy as jnp
from jax import lax
from jax.sharding import PartitionSpec as P

STEPS = 3
ALL = ("sens", "freq")


def circulant(taps):
    n = taps.shape[0]
    nb = 128
    row = lax.broadcasted_iota(jnp.int32, (nb, n), 0)
    band = jnp.broadcast_to(taps[None, :], (nb, n))
    for bit in range(7):
        band = jnp.where(((row >> bit) & 1) == 1, jnp.roll(band, 1 << bit, axis=1), band)
    band = band.astype(jnp.bfloat16)
    return jnp.concatenate([jnp.roll(band, nb * a, axis=1) for a in range(n // nb)], axis=0)


def split(x):
    hi = x.astype(jnp.bfloat16)
    return hi, (x - hi.astype(jnp.float32)).astype(jnp.bfloat16)


def dot_left(a, x):
    hi, lo = split(x)
    f32 = jnp.float32
    return jnp.dot(a, hi, preferred_element_type=f32) + jnp.dot(a, lo, preferred_element_type=f32)


def dot_right(x, b):
    hi, lo = split(x)
    f32 = jnp.float32
    return jnp.dot(hi, b, preferred_element_type=f32) + jnp.dot(lo, b, preferred_element_type=f32)


def rotate_to_source(stacked, me, count):
    doubled = jnp.concatenate([stacked, stacked], axis=0)
    return lax.dynamic_slice_in_dim(doubled, count - me, count, axis=0)


def local(residual, spec_gain, factor_panel, diag_inverse):
    nf = lax.axis_size("freq")
    ns = lax.axis_size("sens")
    fi = lax.axis_index("freq")
    si = lax.axis_index("sens")
    pos = si * nf + fi
    block = factor_panel.shape[0]
    tl = residual.shape[1]
    n = tl * nf
    head = STEPS * block
    f32, bf16 = jnp.float32, jnp.bfloat16

    taps = jnp.fft.irfft(spec_gain, n=n).astype(f32)
    kernel = circulant(taps)

    own = lax.all_to_all(residual, "freq", split_axis=0, concat_axis=1, tiled=True)
    field = jnp.dot(own, kernel, preferred_element_type=f32)

    piece = block // nf
    cols = (STEPS - 1) * block
    got = []
    for d in range(1, nf):
        start = ((fi + d) % nf) * piece
        mine = lax.dynamic_slice_in_dim(factor_panel, start, piece, axis=0)[:, :cols]
        pairs = [(src, (src + d) % nf) for src in range(1, STEPS)]
        got.append(lax.ppermute(mine, ALL, pairs))
    own_piece = lax.dynamic_slice_in_dim(factor_panel, fi * piece, piece, axis=0)[:, :cols]
    part1 = jnp.where(fi == 1, own_piece, 0).astype(bf16)
    part2 = jnp.where(fi == 2, own_piece, 0).astype(bf16)
    for d in range(1, nf):
        part1 = part1 + jnp.where(fi == (1 + d) % nf, got[d - 1], 0).astype(bf16)
        part2 = part2 + jnp.where(fi == (2 + d) % nf, got[d - 1], 0).astype(bf16)
    mixed = jnp.concatenate([part1[:, :block], part2], axis=1)
    stacked = [mixed]
    for d in range(1, nf):
        pairs = [(j, (j - d) % nf) for j in range(nf)]
        stacked.append(lax.ppermute(mixed, ALL, pairs))
    panels = jnp.stack(stacked).reshape(nf * piece, STEPS * block)
    p10 = panels[:, :block]
    p20 = panels[:, block : 2 * block]
    p21 = panels[:, 2 * block :]

    own, headrows = lax.optimization_barrier((own, residual[:head]))
    rows = [headrows[k * block : (k + 1) * block] for k in range(STEPS)]
    inv = [diag_inverse[k * block : (k + 1) * block] for k in range(STEPS)]
    def turn(x, axis):
        return lax.dynamic_slice_in_dim(jnp.concatenate([x, x], axis=axis), fi * piece, block, axis=axis)

    y0 = jnp.dot(inv[0], rows[0], preferred_element_type=f32)
    z1 = turn(rows[1], 0).astype(f32) - dot_left(p10, y0)
    y1 = dot_left(turn(inv[1], 1), z1)
    z2 = turn(rows[2], 0).astype(f32) - dot_left(p20, y0) - dot_left(p21, y1)
    y2 = dot_left(turn(inv[2], 1), z2)
    ys = jnp.concatenate([y0, y1, y2], axis=0)

    rs = head // ns
    mine = ys[:rs]
    for s in range(1, ns):
        recv = lax.ppermute(ys[s * rs : (s + 1) * rs], ALL, [(f, s * nf + f) for f in range(nf)])
        mine = jnp.where(si == s, recv, mine)
    copies = jnp.broadcast_to(mine[None], (nf, rs, tl))
    yrows = lax.all_to_all(copies, "freq", 0, 0, tiled=False)
    yrows = jnp.transpose(yrows, (1, 0, 2)).reshape(rs, n)
    srows = dot_right(yrows, kernel).astype(bf16)
    solved = lax.all_gather(srows, "sens", axis=0, tiled=True)

    update = jnp.dot(factor_panel, solved, preferred_element_type=f32)
    rest = (field - update).astype(bf16)
    step_rows = lax.dynamic_slice_in_dim(solved, jnp.minimum(pos, STEPS - 1) * block, block, axis=0)
    return jnp.where(pos < STEPS, step_rows, rest)


def solution(mesh):
    in_specs = (P("sens", "freq"), P(), P(("sens", "freq"), None), P())
    out_specs = P(("sens", "freq"), None)
    return jax.shard_map(local, mesh=mesh, in_specs=in_specs, out_specs=out_specs, check_vma=False)
```
